256 devices in a mesh: tok: 64 (over x_hi, z, y), ffn: 4 (over x_lo, core).
Axes of the slice: x: 4 (x_hi: 2, x_lo: 2; x = x_hi * 2 + x_lo), y: 4, z: 8, core: 2. Of those that a mesh axis runs over, the one named last changes fastest.
Arguments:
- hidden: bfloat16 [65536, 8192], P('tok', 'ffn'), may hold values from -6 to 6
- down_weight: bfloat16 [2, 3072, 8192], P(None, 'tok', 'ffn'), may hold values from -0.0625 to 0.0625
- block_expert: int32 [512], P('tok'), may hold values from 0 to 1, as said below
- slot_token: int32 [65536], P('tok'), may hold values from 0 to 512, as said below
- slot_weight: float32 [65536], P('tok'), may hold values from 0.1 to 1
Outputs:
- mixed: bfloat16 [32768, 3072], P('tok', 'ffn')
The draws below stay inside these ranges and needn't reach their ends.
Inputs may be any that keep to these rules, and one draw needn't show every extreme that they name: `slot_token`: within each index of tok, slots 128 * b to 128 * b + 127 belong to expert block_expert of block b; each expert's blocks are consecutive, in expert order, with its live slots first; live slots of one expert hold distinct tokens; the value 512 marks an empty slot; one index of tok has at most 512 live slots for one expert, and for every expert some index has exactly that many. `block_expert`: every expert owns at least one block of every index of tok; blocks after the last expert's live slots carry the last expert.
All inputs are finite; a program needn't handle non-finite values.
Results may differ from the reference program's by a relative error of at most 0.001.
Values may be sent and summed in bfloat16 or wider, within the bound.
No kernel may reach another device: no remote copies, remote signals or barrier semaphores. Data moves between devices by JAX's collectives and lax.ppermute only.
A program may use at most 128 MiB of HBM per device.

```python
import jax
import jax.numpy as jnp
from jax import lax

D = 3072
FF = 8192
EXP = 2
BLOCK = 128
ROWS_EXP = 512
TOK_DEV = 512
NBLK = 8
SLOTS = 1024
TOKENS = 32768
N_TOK = 64


def layout_tables(key):
    base = jax.random.fold_in(key, 4711)
    key_count, key_full, key_order = jax.random.split(base, 3)
    devices = TOKENS // TOK_DEV
    counts = jax.random.randint(key_count, (devices, EXP), ROWS_EXP // 4, ROWS_EXP + 1)
    full_dev = jax.random.randint(key_full, (EXP,), 0, devices)
    counts = jnp.where(jnp.arange(devices)[:, None] == full_dev[None, :], ROWS_EXP, counts)
    order_keys = jax.random.split(key_order, devices * EXP)
    orders = jax.vmap(lambda subkey: jax.random.permutation(subkey, TOK_DEV))(order_keys)
    orders = orders.reshape(devices, EXP, TOK_DEV)
    needed = (counts + BLOCK - 1) // BLOCK
    starts = jnp.cumsum(needed, axis=1) - needed
    slot_ids = jnp.arange(NBLK * BLOCK)
    block_of = slot_ids // BLOCK
    within = slot_ids % BLOCK
    owners = jnp.sum((block_of[None, None, :] >= starts[:, :, None]).astype(jnp.int32), axis=1) - 1
    start_of = jnp.take_along_axis(starts, owners, axis=1)
    count_of = jnp.take_along_axis(counts, owners, axis=1)
    rank_in = (block_of[None, :] - start_of) * BLOCK + within[None, :]
    is_live = rank_in < count_of
    token_ids = orders[jnp.arange(devices)[:, None], owners, jnp.minimum(rank_in, TOK_DEV - 1)]
    slot_tokens = jnp.where(is_live, token_ids, TOK_DEV).astype(jnp.int32)
    block_experts = owners[:, ::BLOCK].astype(jnp.int32)
    return (slot_tokens.reshape(-1), block_experts.reshape(-1))


def draw_slot_token(key, part):
    return layout_tables(key)[0]


def draw_block_expert(key, part):
    return layout_tables(key)[1]


def shard_levels(key, dims, cuts, low, largest):
    gain, own = 1.0, jax.random.fold_in(key, 6)
    for dim, parts in cuts:
        steps = jnp.exp(jax.random.uniform(jax.random.fold_in(own, dim), (parts,), jnp.float32, low / len(cuts), largest / len(cuts)))
        gain = gain * jnp.repeat(steps, dims[dim] // parts).reshape([-1 if axis == dim else 1 for axis in range(len(dims))])
    return gain


def bell_draw(stream_key, shape, scale, bound, cuts=(), held_as=jnp.bfloat16):
    loudness = shard_levels(stream_key, shape, cuts, -0.22, 0.18) if cuts else 1.0
    result = jax.random.normal(stream_key, shape, jnp.float32) * scale * loudness
    return jnp.minimum(jnp.maximum(result, -bound), bound).astype(held_as)


def setup_inputs(seed: int = 0) -> dict:
    streams_of = jax.random.split(jax.random.key(seed), 6)
    return {
        "hidden": bell_draw(streams_of[0], (N_TOK * SLOTS, FF), 1.0, 6.0, ((0, 64), (1, 4))),
        "down_weight": bell_draw(streams_of[1], (EXP, D, FF), FF ** -0.5, 0.0625, ((1, 64), (2, 4))),
        "block_expert": draw_block_expert(jax.random.fold_in(streams_of[5], 71), 0),
        "slot_token": draw_slot_token(jax.random.fold_in(streams_of[5], 71), 0),
        "slot_weight": jnp.clip(0.1 + 0.9 * jax.random.uniform(streams_of[4], (N_TOK * SLOTS,), jnp.float32) ** shard_levels(streams_of[4], (N_TOK * SLOTS,), ((0, 64),), -0.2, 0.2), 0.1, 1.0),
    }


def reference(hidden, down_weight, block_expert, slot_token, slot_weight):
    devices = TOKENS // TOK_DEV
    hidden_dev = hidden.reshape(devices, SLOTS, FF)
    expert_dev = block_expert.reshape(devices, NBLK)
    token_dev = slot_token.reshape(devices, SLOTS)
    weight_dev = slot_weight.reshape(devices, SLOTS)

    def one_device(packed):
        hidden_one, expert_one, token_one, weight_one = packed
        block_outs = []
        for block_idx in range(NBLK):
            weight_panel = lax.dynamic_index_in_dim(down_weight, expert_one[block_idx], 0, keepdims=False)
            hblock = hidden_one[block_idx * BLOCK:(block_idx + 1) * BLOCK]
            block_outs.append(lax.dot_general(hblock, weight_panel, (((1,), (1,)), ((), ())), preferred_element_type=jnp.float32))
        slot_out = jnp.concatenate(block_outs, axis=0)
        is_live = token_one < TOK_DEV
        slot_scale = jnp.where(is_live, weight_one, jnp.zeros_like(weight_one))
        token_slot = jnp.minimum(token_one, TOK_DEV - 1).astype(jnp.int32)
        summed = jax.ops.segment_sum(slot_scale[:, None] * slot_out, token_slot, num_segments=TOK_DEV)
        return summed.astype(jnp.bfloat16)

    mixed = lax.map(one_device, (hidden_dev, expert_dev, token_dev, weight_dev))
    return mixed.reshape(TOKENS, D)
```

```python
import jax
import jax.numpy as jnp
from jax import lax
from jax.sharding import Mesh, PartitionSpec as P

EXP = 2
BLOCK = 128
TOK_DEV = 512

TOK = ("xh", "z", "y")
FFN = ("xl", "c")


def local(hidden, down_weight, block_expert, slot_token, slot_weight):
    halves = lax.all_gather(down_weight, "xh", axis=0, tiled=False)
    w_full = lax.all_gather(halves, ("z", "y"), axis=2, tiled=True)
    slot_expert = jnp.repeat(block_expert, BLOCK)
    tokens = jnp.arange(TOK_DEV, dtype=jnp.int32)
    same_token = slot_token[None, :] == tokens[:, None]
    token_terms = None
    for number in range(EXP):
        pick = same_token & (slot_expert == number)[None, :]
        scale = jnp.sum(jnp.where(pick, slot_weight[None, :], 0.0), axis=1)
        rows = lax.dot_general(
            pick.astype(hidden.dtype), hidden, (((1,), (0,)), ((), ())),
            preferred_element_type=jnp.float32,
        ).astype(hidden.dtype)
        out = lax.dot_general(
            rows, w_full[:, number], (((1,), (2,)), ((), ())),
            preferred_element_type=jnp.float32,
        )
        term = scale[:, None] * out.reshape(TOK_DEV, -1)
        token_terms = term if token_terms is None else token_terms + term
    mixed = lax.psum_scatter(token_terms, FFN, scatter_dimension=1, tiled=True)
    return mixed.astype(jnp.bfloat16)


def solution(mesh):
    tok_size, ffn_size = mesh.devices.shape
    fine = Mesh(mesh.devices.reshape(2, tok_size // 8, 4, 2, ffn_size // 2), TOK + FFN)
    placed = (P(TOK, FFN), P(None, TOK, FFN), P(TOK), P(TOK), P(TOK))
    return jax.shard_map(
        local, mesh=fine, in_specs=placed, out_specs=P(TOK, FFN), check_vma=False
    )
```

```python
import jax
import jax.numpy as jnp
from jax import lax
from jax.sharding import Mesh, PartitionSpec as P

EXP = 2
BLOCK = 128
TOK_DEV = 512

TOK = ("xh", "z", "y")
FFN = ("xl", "c")


def half_terms(rows, scale, w_half):
    out = lax.dot_general(
        rows, w_half, (((2,), (2,)), ((0,), (0,))), preferred_element_type=jnp.float32
    )
    return jnp.sum(scale[:, :, None] * out, axis=0)


def local(hidden, down_weight, block_expert, slot_token, slot_weight):
    own_half = lax.all_gather(down_weight, ("z", "y"), axis=1, tiled=True)
    partner = lax.ppermute(down_weight, "xh", perm=[(0, 1), (1, 0)])
    other_half = lax.all_gather(partner, ("z", "y"), axis=1, tiled=True)
    slot_expert = jnp.repeat(block_expert, BLOCK)
    tokens = jnp.arange(TOK_DEV, dtype=jnp.int32)
    experts = jnp.arange(EXP, dtype=jnp.int32)
    pick = (slot_token[None, None, :] == tokens[None, :, None]) & (
        slot_expert[None, None, :] == experts[:, None, None]
    )
    scale = jnp.sum(jnp.where(pick, slot_weight[None, None, :], 0.0), axis=2)
    rows = lax.dot_general(
        pick.astype(hidden.dtype), hidden, (((2,), (0,)), ((), ())),
        preferred_element_type=jnp.float32,
    ).astype(hidden.dtype)
    own_terms = half_terms(rows, scale, own_half)
    other_terms = half_terms(rows, scale, other_half)
    first = lax.axis_index("xh") == 0
    token_terms = jnp.concatenate(
        [jnp.where(first, own_terms, other_terms), jnp.where(first, other_terms, own_terms)], axis=1
    )
    mixed = lax.psum_scatter(token_terms, FFN, scatter_dimension=1, tiled=True)
    return mixed.astype(jnp.bfloat16)


def solution(mesh):
    tok_size, ffn_size = mesh.devices.shape
    fine = Mesh(mesh.devices.reshape(2, tok_size // 8, 4, 2, ffn_size // 2), TOK + FFN)
    placed = (P(TOK, FFN), P(None, TOK, FFN), P(TOK), P(TOK), P(TOK))
    return jax.shard_map(
        local, mesh=fine, in_specs=placed, out_specs=P(TOK, FFN), check_vma=False
    )
```

```python
import jax
import jax.numpy as jnp
from jax import lax
from jax.sharding import Mesh, PartitionSpec as P

EXP = 2
BLOCK = 128
TOK_DEV = 512

TOK = ("xh", "z", "y")
FFN = ("xl", "c")
SWAP = [(0, 1), (1, 0)]


def halve(terms, axis, name):
    own = lax.axis_index(name)
    keep = lax.dynamic_index_in_dim(terms, own, axis=axis, keepdims=False)
    send = lax.dynamic_index_in_dim(terms, 1 - own, axis=axis, keepdims=False)
    return keep + lax.ppermute(send, name, perm=SWAP)


def local(hidden, down_weight, block_expert, slot_token, slot_weight):
    partner = lax.ppermute(down_weight, "xh", perm=SWAP)
    first = lax.axis_index("xh") == 0
    pair = jnp.stack(
        [jnp.where(first, down_weight, partner), jnp.where(first, partner, down_weight)], axis=0
    )
    w_full = lax.all_gather(pair, ("z", "y"), axis=2, tiled=True)
    slot_expert = jnp.repeat(block_expert, BLOCK)
    tokens = jnp.arange(TOK_DEV, dtype=jnp.int32)
    experts = jnp.arange(EXP, dtype=jnp.int32)
    pick = (slot_token[None, None, :] == tokens[None, :, None]) & (
        slot_expert[None, None, :] == experts[:, None, None]
    )
    scale = jnp.sum(jnp.where(pick, slot_weight[None, None, :], 0.0), axis=2)
    rows = lax.dot_general(
        pick.astype(hidden.dtype), hidden, (((2,), (0,)), ((), ())),
        preferred_element_type=jnp.float32,
    ).astype(hidden.dtype)
    out = lax.dot_general(
        rows, w_full, (((2,), (3,)), ((0,), (1,))), preferred_element_type=jnp.float32
    )
    token_terms = jnp.sum(scale[:, :, None, None] * out, axis=0)
    half = token_terms.shape[2]
    token_terms = token_terms.reshape(TOK_DEV, 2, 2, half // 2).transpose(1, 2, 0, 3)
    mixed = halve(halve(token_terms, 1, "c"), 0, "xl")
    return mixed.astype(jnp.bfloat16)


def solution(mesh):
    tok_size, ffn_size = mesh.devices.shape
    fine = Mesh(mesh.devices.reshape(2, tok_size // 8, 4, 2, ffn_size // 2), TOK + FFN)
    placed = (P(TOK, FFN), P(None, TOK, FFN), P(TOK), P(TOK), P(TOK))
    return jax.shard_map(
        local, mesh=fine, in_specs=placed, out_specs=P(TOK, FFN), check_vma=False
    )
```

```python
import jax
import jax.numpy as jnp
from jax import lax
from jax.sharding import Mesh, PartitionSpec as P

EXP = 2
BLOCK = 128
TOK_DEV = 512

TOK = ("xh", "z", "y")
FFN = ("xl", "c")
SWAP = [(0, 1), (1, 0)]


def local(hidden, down_weight, block_expert, slot_token, slot_weight):
    partner = lax.ppermute(down_weight, "xh", perm=SWAP)
    first = lax.axis_index("xh") == 0
    pair = jnp.stack(
        [jnp.where(first, down_weight, partner), jnp.where(first, partner, down_weight)], axis=0
    )
    w_full = lax.all_gather(pair, ("z", "y"), axis=2, tiled=True)
    slot_expert = jnp.repeat(block_expert, BLOCK)
    tokens = jnp.arange(TOK_DEV, dtype=jnp.int32)
    experts = jnp.arange(EXP, dtype=jnp.int32)
    pick = (slot_token[None, None, :] == tokens[None, :, None]) & (
        slot_expert[None, None, :] == experts[:, None, None]
    )
    scale = jnp.sum(jnp.where(pick, slot_weight[None, None, :], 0.0), axis=2)
    rows = lax.dot_general(
        pick.astype(hidden.dtype), hidden, (((2,), (0,)), ((), ())),
        preferred_element_type=jnp.float32,
    ).astype(hidden.dtype)
    rows, scale = lax.optimization_barrier((rows, scale))
    quarter = w_full.shape[2] // 2
    xl, c = lax.axis_index("xl"), lax.axis_index("c")

    def terms(h, part):
        w_part = lax.dynamic_slice_in_dim(w_full[h], part * quarter, quarter, axis=1)
        out = lax.dot_general(
            rows, w_part, (((2,), (2,)), ((0,), (0,))), preferred_element_type=jnp.float32
        )
        return jnp.sum(scale[:, :, None] * out, axis=0)

    def by_core(h):
        sent = lax.ppermute(terms(h, 1 - c), "c", perm=SWAP)
        return terms(h, c) + sent

    far = lax.ppermute(by_core(1 - xl), "xl", perm=SWAP)
    mixed = by_core(xl) + far
    return mixed.astype(jnp.bfloat16)


def solution(mesh):
    tok_size, ffn_size = mesh.devices.shape
    fine = Mesh(mesh.devices.reshape(2, tok_size // 8, 4, 2, ffn_size // 2), TOK + FFN)
    placed = (P(TOK, FFN), P(None, TOK, FFN), P(TOK), P(TOK), P(TOK))
    return jax.shard_map(
        local, mesh=fine, in_specs=placed, out_specs=P(TOK, FFN), check_vma=False
    )
```

```python
import jax
import jax.numpy as jnp
from jax import lax
from jax.sharding import Mesh, PartitionSpec as P


EXP = 2
BLOCK = 128
TOK_DEV = 512
CHUNKS = 2

TOK = ("xh", "z", "y")
FFN = ("xl", "c")
SWAP = [(0, 1), (1, 0)]


def body(hidden, down_weight, block_expert, slot_token, slot_weight):
    partner = lax.ppermute(down_weight, "xh", perm=SWAP)
    first = lax.axis_index("xh") == 0
    pair = jnp.stack(
        [jnp.where(first, down_weight, partner), jnp.where(first, partner, down_weight)], axis=0
    )
    w_full = lax.all_gather(pair, ("z", "y"), axis=2, tiled=True)
    slot_expert = jnp.repeat(block_expert, BLOCK)
    tokens = jnp.arange(TOK_DEV, dtype=jnp.int32)
    experts = jnp.arange(EXP, dtype=jnp.int32)
    pick = (slot_token[None, None, :] == tokens[None, :, None]) & (
        slot_expert[None, None, :] == experts[:, None, None]
    )
    scale = jnp.sum(jnp.where(pick, slot_weight[None, None, :], 0.0), axis=2)
    rows = lax.dot_general(
        pick.astype(hidden.dtype), hidden, (((2,), (0,)), ((), ())),
        preferred_element_type=jnp.float32,
    ).astype(hidden.dtype)
    rows, scale = lax.optimization_barrier((rows, scale))
    quarter = w_full.shape[2] // 2
    xl, c = lax.axis_index("xl"), lax.axis_index("c")

    def terms(rows, scale, h, part):
        w_part = lax.dynamic_slice_in_dim(w_full[h], part * quarter, quarter, axis=1)
        out = lax.dot_general(
            rows, w_part, (((2,), (2,)), ((0,), (0,))), preferred_element_type=jnp.float32
        )
        return jnp.sum(scale[:, :, None] * out, axis=0)

    def by_core(rows, scale, h):
        sent = lax.ppermute(terms(rows, scale, h, 1 - c), "c", perm=SWAP)
        return terms(rows, scale, h, c) + sent

    chunk = TOK_DEV // CHUNKS
    far = []
    for k in range(CHUNKS):
        part = slice(k * chunk, (k + 1) * chunk)
        far.append(by_core(rows[:, part], scale[:, part], 1 - xl))
    near_rows, near_scale, *far = lax.optimization_barrier((rows, scale, *far))
    far = [lax.ppermute(piece, "xl", perm=SWAP) for piece in far]
    near = by_core(near_rows, near_scale, xl)
    mixed = near + jnp.concatenate(far, axis=0)
    return mixed.astype(jnp.bfloat16)


def solution(mesh):
    tok_size, ffn_size = mesh.devices.shape
    fine = Mesh(mesh.devices.reshape(2, tok_size // 8, 4, 2, ffn_size // 2), TOK + FFN)
    placed = (P(TOK, FFN), P(None, TOK, FFN), P(TOK), P(TOK), P(TOK))
    return jax.shard_map(body, mesh=fine, in_specs=placed, out_specs=P(TOK, FFN), check_vma=False)
```

```python
import jax
import jax.numpy as jnp
from jax import lax
from jax.sharding import Mesh, PartitionSpec as P


EXP = 2
BLOCK = 128
TOK_DEV = 512

TOK = ("xh", "z", "y")
FFN = ("xl", "c")
SWAP = [(0, 1), (1, 0)]


def body(hidden, down_weight, block_expert, slot_token, slot_weight):
    partner = lax.ppermute(down_weight, "xh", perm=SWAP)
    pair = jnp.stack([down_weight, partner], axis=0)
    w_full = lax.all_gather(pair, ("z", "y"), axis=2, tiled=True)
    xh = lax.axis_index("xh")
    slot_expert = jnp.repeat(block_expert, BLOCK)
    tokens = jnp.arange(TOK_DEV, dtype=jnp.int32)
    experts = jnp.arange(EXP, dtype=jnp.int32)
    pick = (slot_token[None, None, :] == tokens[None, :, None]) & (
        slot_expert[None, None, :] == experts[:, None, None]
    )
    scale = jnp.sum(jnp.where(pick, slot_weight[None, None, :], 0.0), axis=2)
    rows = lax.dot_general(
        pick.astype(hidden.dtype), hidden, (((2,), (0,)), ((), ())),
        preferred_element_type=jnp.float32,
    ).astype(hidden.dtype)
    rows, scale = lax.optimization_barrier((rows, scale))
    quarter = w_full.shape[2] // 2
    xl, c = lax.axis_index("xl"), lax.axis_index("c")

    def terms(rows, scale, h, part):
        w_part = lax.dynamic_slice_in_dim(w_full[(h + xh) % 2], part * quarter, quarter, axis=1)
        out = lax.dot_general(
            rows, w_part, (((2,), (2,)), ((0,), (0,))), preferred_element_type=jnp.float32
        )
        return jnp.sum(scale[:, :, None] * out, axis=0)

    def by_core(rows, scale, h):
        sent = lax.ppermute(terms(rows, scale, h, 1 - c), "c", perm=SWAP)
        return terms(rows, scale, h, c) + sent

    far = by_core(rows, scale, 1 - xl)
    near_rows, near_scale, far = lax.optimization_barrier((rows, scale, far))
    far = lax.ppermute(far, "xl", perm=SWAP)
    near = by_core(near_rows, near_scale, xl)
    mixed = near + far
    return mixed.astype(jnp.bfloat16)


def solution(mesh):
    tok_size, ffn_size = mesh.devices.shape
    fine = Mesh(mesh.devices.reshape(2, tok_size // 8, 4, 2, ffn_size // 2), TOK + FFN)
    placed = (P(TOK, FFN), P(None, TOK, FFN), P(TOK), P(TOK), P(TOK))
    return jax.shard_map(body, mesh=fine, in_specs=placed, out_specs=P(TOK, FFN), check_vma=False)
```

```python
import jax
import jax.numpy as jnp
from jax import lax
from jax.sharding import Mesh, PartitionSpec as P


EXP = 2
BLOCK = 128
TOK_DEV = 512

TOK = ("xh", "z", "y")
FFN = ("xl", "c")
SWAP = [(0, 1), (1, 0)]


def body(hidden, down_weight, block_expert, slot_token, slot_weight):
    partner = lax.ppermute(down_weight, "xh", perm=SWAP)
    pair = jnp.stack([down_weight, partner], axis=0)
    w_full = lax.all_gather(pair, ("z", "y"), axis=2, tiled=True)
    xh = lax.axis_index("xh")
    slot_expert = jnp.repeat(block_expert, BLOCK)
    tokens = jnp.arange(TOK_DEV, dtype=jnp.int32)
    experts = jnp.arange(EXP, dtype=jnp.int32)
    pick = (slot_token[None, None, :] == tokens[None, :, None]) & (
        slot_expert[None, None, :] == experts[:, None, None]
    )
    scale = jnp.sum(jnp.where(pick, slot_weight[None, None, :], 0.0), axis=2)
    rows = lax.dot_general(
        pick.astype(hidden.dtype), hidden, (((2,), (0,)), ((), ())),
        preferred_element_type=jnp.float32,
    ).astype(hidden.dtype)
    rows, scale = lax.optimization_barrier((rows, scale))
    quarter = w_full.shape[2] // 2
    xl, c = lax.axis_index("xl"), lax.axis_index("c")

    def terms(rows, scale, h, part, lo=0, size=quarter):
        w_part = lax.dynamic_slice_in_dim(w_full[(h + xh) % 2], part * quarter + lo, size, axis=1)
        out = lax.dot_general(
            rows, w_part, (((2,), (2,)), ((0,), (0,))), preferred_element_type=jnp.float32
        )
        return jnp.sum(scale[:, :, None] * out, axis=0)

    def by_core(rows, scale, h, lo=0, size=quarter):
        sent = lax.ppermute(terms(rows, scale, h, 1 - c, lo, size), "c", perm=SWAP)
        return terms(rows, scale, h, c, lo, size) + sent

    widths = (quarter // 6, quarter // 3)
    widths = widths + (quarter - sum(widths),)
    sent_far, lo = [], 0
    for width in widths:
        piece = by_core(rows, scale, 1 - xl, lo, width)
        sent_far.append(lax.ppermute(piece, "xl", perm=SWAP))
        rows, scale, piece = lax.optimization_barrier((rows, scale, piece))
        lo += width
    near_rows, near_scale = rows, scale
    near = by_core(near_rows, near_scale, xl)
    mixed = near + jnp.concatenate(sent_far, axis=1)
    return mixed.astype(jnp.bfloat16)


def solution(mesh):
    tok_size, ffn_size = mesh.devices.shape
    fine = Mesh(mesh.devices.reshape(2, tok_size // 8, 4, 2, ffn_size // 2), TOK + FFN)
    placed = (P(TOK, FFN), P(None, TOK, FFN), P(TOK), P(TOK), P(TOK))
    return jax.shard_map(body, mesh=fine, in_specs=placed, out_specs=P(TOK, FFN), check_vma=False)
```

```python
import jax
import jax.numpy as jnp
from jax import lax
from jax.sharding import Mesh, PartitionSpec as P


EXP = 2
BLOCK = 128
TOK_DEV = 512

TOK = ("xh", "z", "y")
FFN = ("xl", "c")
SWAP = [(0, 1), (1, 0)]


def body(hidden, down_weight, block_expert, slot_token, slot_weight):
    partner = lax.ppermute(down_weight, "xh", perm=SWAP)
    pair = jnp.stack([down_weight, partner], axis=0)
    w_full = lax.all_gather(pair, ("z", "y"), axis=2, tiled=True)
    xh = lax.axis_index("xh")
    slot_expert = jnp.repeat(block_expert, BLOCK)
    tokens = jnp.arange(TOK_DEV, dtype=jnp.int32)
    experts = jnp.arange(EXP, dtype=jnp.int32)
    pick = (slot_token[None, None, :] == tokens[None, :, None]) & (
        slot_expert[None, None, :] == experts[:, None, None]
    )
    scale = jnp.sum(jnp.where(pick, slot_weight[None, None, :], 0.0), axis=2)
    rows = lax.dot_general(
        pick.astype(hidden.dtype), hidden, (((2,), (0,)), ((), ())),
        preferred_element_type=jnp.float32,
    ).astype(hidden.dtype)
    rows, scale = lax.optimization_barrier((rows, scale))
    quarter = w_full.shape[2] // 2
    xl, c = lax.axis_index("xl"), lax.axis_index("c")

    def terms(rows, scale, h, part, lo=0, size=quarter):
        w_part = lax.dynamic_slice_in_dim(w_full[(h + xh) % 2], part * quarter + lo, size, axis=1)
        out = lax.dot_general(
            rows, w_part, (((2,), (2,)), ((0,), (0,))), preferred_element_type=jnp.float32
        )
        return jnp.sum(scale[:, :, None] * out, axis=0)

    def by_core(rows, scale, h, lo=0, size=quarter):
        sent = lax.ppermute(terms(rows, scale, h, 1 - c, lo, size), "c", perm=SWAP)
        return terms(rows, scale, h, c, lo, size) + sent

    piece = quarter // 3
    first = by_core(rows, scale, 1 - xl, 0, piece)
    first_far = lax.ppermute(first, "xl", perm=SWAP)
    rows, scale, first = lax.optimization_barrier((rows, scale, first))
    second = by_core(rows, scale, 1 - xl, piece, quarter - piece)
    near_rows, near_scale, second = lax.optimization_barrier((rows, scale, second))
    second_far = lax.ppermute(second, "xl", perm=SWAP)
    near = by_core(near_rows, near_scale, xl)
    mixed = [
        (near[:, :piece] + first_far).astype(jnp.bfloat16),
        (near[:, piece:] + second_far).astype(jnp.bfloat16),
    ]
    return jnp.concatenate(mixed, axis=1)


def solution(mesh):
    tok_size, ffn_size = mesh.devices.shape
    fine = Mesh(mesh.devices.reshape(2, tok_size // 8, 4, 2, ffn_size // 2), TOK + FFN)
    placed = (P(TOK, FFN), P(None, TOK, FFN), P(TOK), P(TOK), P(TOK))
    return jax.shard_map(body, mesh=fine, in_specs=placed, out_specs=P(TOK, FFN), check_vma=False)
```

```python
import jax
import jax.numpy as jnp
from jax import lax
from jax.sharding import Mesh, PartitionSpec as P


EXP = 2
BLOCK = 128
TOK_DEV = 512

TOK = ("xh", "z", "y")
FFN = ("xl", "c")
SWAP = [(0, 1), (1, 0)]


def body(hidden, down_weight, block_expert, slot_token, slot_weight):
    partner = lax.ppermute(down_weight, "xh", perm=SWAP)
    pair = jnp.stack([down_weight, partner], axis=0)
    w_full = lax.all_gather(pair, ("z", "y"), axis=2, tiled=True)
    xh = lax.axis_index("xh")
    slot_expert = jnp.repeat(block_expert, BLOCK)
    tokens = jnp.arange(TOK_DEV, dtype=jnp.int32)
    experts = jnp.arange(EXP, dtype=jnp.int32)
    pick = (slot_token[None, None, :] == tokens[None, :, None]) & (
        slot_expert[None, None, :] == experts[:, None, None]
    )
    scale = jnp.sum(jnp.where(pick, slot_weight[None, None, :], 0.0), axis=2)
    rows = lax.dot_general(
        pick.astype(hidden.dtype), hidden, (((2,), (0,)), ((), ())),
        preferred_element_type=jnp.float32,
    ).astype(hidden.dtype)
    rows, scale = lax.optimization_barrier((rows, scale))
    quarter = w_full.shape[2] // 2
    xl, c = lax.axis_index("xl"), lax.axis_index("c")

    def terms(rows, scale, h, part, lo=0, size=quarter):
        w_part = lax.dynamic_slice_in_dim(w_full[(h + xh) % 2], part * quarter + lo, size, axis=1)
        out = lax.dot_general(
            rows, w_part, (((2,), (2,)), ((0,), (0,))), preferred_element_type=jnp.float32
        )
        return jnp.sum(scale[:, :, None] * out, axis=0)

    def by_core(rows, scale, h, lo=0, size=quarter):
        sent = lax.ppermute(terms(rows, scale, h, 1 - c, lo, size), "c", perm=SWAP)
        return terms(rows, scale, h, c, lo, size) + sent

    piece = quarter // 6
    first = by_core(rows, scale, 1 - xl, 0, piece)
    first_far = lax.ppermute(first, "xl", perm=SWAP)
    rows, scale, first = lax.optimization_barrier((rows, scale, first))
    second = by_core(rows, scale, 1 - xl, piece, quarter - piece)
    near_rows, near_scale, second = lax.optimization_barrier((rows, scale, second))
    second_far = lax.ppermute(second, "xl", perm=SWAP)
    near = by_core(near_rows, near_scale, xl)
    mixed = near + jnp.concatenate([first_far, second_far], axis=1)
    return mixed.astype(jnp.bfloat16)


def solution(mesh):
    tok_size, ffn_size = mesh.devices.shape
    fine = Mesh(mesh.devices.reshape(2, tok_size // 8, 4, 2, ffn_size // 2), TOK + FFN)
    placed = (P(TOK, FFN), P(None, TOK, FFN), P(TOK), P(TOK), P(TOK))
    return jax.shard_map(body, mesh=fine, in_specs=placed, out_specs=P(TOK, FFN), check_vma=False)
```
